256 devices in a mesh: blk: 4 (over x), shard: 64 (over y, z, core).
Axes of the slice: x: 4, y: 4, z: 8, core: 2. Of those that a mesh axis runs over, the one named last changes fastest.
Arguments:
- table: bfloat16 [524288, 400], P(('blk', 'shard')), may hold values from -3 to 3
- relation: bfloat16 [1345, 400], replicated, may hold values from -3 to 3
- owners: int32 [262144, 2], P(('blk', 'shard')), may hold values from 0 to 63, all different within a row; in each aligned block of 1024 rows (0 to 1023, 1024 to 2047, ...) at most 64 rows name the same one
- rows: int32 [262144, 2], P(('blk', 'shard')), may hold values from 0 to 2047
- rel_ids: int32 [262144], P(('blk', 'shard')), may hold values from 0 to 1344
- span_ids: int32 [256], P(('blk', 'shard')), may hold values from 0 to 1
Outputs:
- entity_grad: float32 [524288, 400], P(('blk', 'shard'))
- relation_grad: float32 [1345, 400], replicated
The draws below stay inside these ranges and needn't reach their ends.
Inputs may be any that keep to these rules, and one draw needn't show every extreme that they name: Among the 1024 edges of one device no owner index is named by more than 64 edge ends; an edge's source and target owners differ; ends address rows of the devices with the same blk index.
All inputs are finite; a program needn't handle non-finite values.
Results may differ from the reference program's by a relative error of at most 0.0016.
Values may be sent and summed in bfloat16 or wider, within the bound.
No kernel may reach another device: no remote copies, remote signals or barrier semaphores. Data moves between devices by JAX's collectives and lax.ppermute only.
A program may use at most 128 MiB of HBM per device.

```python
import math
import jax
import jax.numpy as jnp
import numpy as np
from jax import lax

D = 400
REL = 1345
NEG = 1024
E_DEV = 1024
ROWS_OWN = 2048
CAP = 64
EDGES = 262144
ENT = 524288
N_BLK = 4
N_SHARD = 64


def touch_ends(values, key, least, largest):
    extent = values.shape
    index_at = [jax.random.randint(jax.random.fold_in(key, axis), (), 0, extent[axis]) for axis in range(len(extent))]
    values = values.at[tuple(index_at)].set(least)
    longest = extent.index(max(extent))
    index_at[longest] = (index_at[longest] + 1) % extent[longest]
    return values.at[tuple(index_at)].set(largest)


def level_of(stream_key, dims, pieces, least, top_value):
    gain, own = 1.0, jax.random.fold_in(stream_key, 6)
    for axis_at, blocks in pieces:
        steps = jnp.exp(jax.random.uniform(jax.random.fold_in(own, axis_at), (blocks,), jnp.float32, least / len(pieces), top_value / len(pieces)))
        gain = gain * jnp.repeat(steps, dims[axis_at] // blocks).reshape([-1 if axis == axis_at else 1 for axis in range(len(dims))])
    return gain


def rank_bounds(count, skew):
    portions = [(1 << 20) // math.isqrt(rank ** skew) + 1 for rank in range(1, count + 1)]
    deviation = 1 + sum(portions) // (1 << 30)
    return np.cumsum(np.array([max(1, weight // deviation) for weight in portions]))


def ranked_ids(stream_key, extent, amount, skew):
    table = rank_bounds(amount, skew)
    pick = jax.random.randint(jax.random.fold_in(stream_key, 1), extent, 0, int(table[amount - 1]))
    grade = jnp.searchsorted(jnp.asarray(table, jnp.int32), pick, side="right")
    return jax.random.permutation(jax.random.fold_in(stream_key, 2), amount)[grade].astype(jnp.int32)


def deal_out(key, own, number, rows, number_of, top, most, slope):
    ranking = jax.random.permutation(key, number_of)
    heavy_load, common = load_shares(number_of, rows * top, most, slope, True), load_shares(number_of, rows * top, most, slope, False)
    places = jnp.arange(number_of)

    def named(tallies, rotation):
        used = int((tallies > 0).sum())
        fixed = max(1, used // 4)
        passed = fixed + (places - fixed + rotation * (used - fixed)) % max(1, number_of - fixed)
        return jnp.zeros((number_of,), jnp.int32).at[ranking[jnp.where(places < fixed, places, passed)]].set(jnp.asarray(tallies, jnp.int32))

    tallies = jnp.where(number % 4 == 0, named(heavy_load, number // 4), named(common, number - number // 4 - 1))
    mixed = jax.random.permutation(jax.random.fold_in(own, 3), number_of)
    source_of, taker = mixed[0:number_of // 2 * 2:2], mixed[1:number_of // 2 * 2:2]
    room = jnp.minimum(tallies[source_of] - 1, most - tallies[taker]) // 2
    room = jnp.where((source_of == ranking[0]) | (taker == ranking[0]) | (tallies[taker] == 0), 0, jnp.maximum(room, 0))
    passed = jax.random.randint(jax.random.fold_in(own, 4), (number_of // 2,), 0, 1 << 20) % (room + 1)
    tallies = tallies.at[source_of].add(-passed).at[taker].add(passed)
    labels = jnp.searchsorted(jnp.cumsum(tallies), jnp.arange(rows * top), side="right").astype(jnp.int32)
    listing = labels.reshape(top, rows).T
    listing = listing[jax.random.permutation(jax.random.fold_in(own, 1), rows)]
    rotation = jax.random.randint(jax.random.fold_in(own, 2), (rows, 1), 0, top)
    return jnp.take_along_axis(listing, (jnp.arange(top)[None, :] + rotation) % top, axis=1)


def load_shares(amount, total, bound, slope, full):
    loads = [(1 << 20) // math.isqrt(standing ** slope) + 1 for standing in range(1, amount + 1)]
    largest = bound if full else min(bound, max(-(-total // amount), total * loads[0] // sum(loads)))
    least = 1 if total - largest >= amount - 1 else 0
    holding, surplus = [largest] + [least] * (amount - 1), total - largest - least * (amount - 1)
    while surplus > 0:
        candidates = [i for i in range(1, amount) if holding[i] < largest] or [i for i in range(1, amount) if holding[i] < bound]
        whole, left = sum([loads[i] for i in candidates]), surplus
        for i in candidates:
            addition = min(bound - holding[i], max(1, left * loads[i] // whole), surplus)
            holding[i] = holding[i] + addition
            surplus = surplus - addition
    return np.array(holding)


def bell_draw(rng, dims, deviation, reach, cuts=(), kind=jnp.bfloat16):
    array = jax.random.normal(rng, dims, jnp.float32) * deviation
    if len(cuts) > 0:
        array = level_of(rng, dims, cuts, -0.22, 0.18) * array
    return jnp.clip(array, min=-reach, max=reach).astype(kind)


def setup_inputs(seed: int = 0) -> dict:
    key_of = jax.random.split(jax.random.key(seed), 7)
    table = bell_draw(key_of[0], (ENT, D), 0.5, 3.0, ((0, 256),))
    relation = bell_draw(key_of[1], (REL, D), 0.5, 3.0)
    owners_keys = jax.random.split(jax.random.fold_in(key_of[2], 1), EDGES // E_DEV)
    owners_turns = jax.random.permutation(jax.random.fold_in(key_of[2], 3), EDGES // E_DEV)
    owners = jax.vmap(lambda own, number: deal_out(jax.random.fold_in(key_of[2], 2), own, number, E_DEV, N_SHARD, 2, CAP, 2))(owners_keys, owners_turns).reshape((EDGES, 2))
    rows = touch_ends(ranked_ids(key_of[3], (EDGES, 2), ROWS_OWN, 2), jax.random.fold_in(key_of[3], 3), 0, ROWS_OWN - 1).astype(jnp.int32)
    rel_ids = touch_ends(ranked_ids(key_of[4], (EDGES,), REL, 2), jax.random.fold_in(key_of[4], 3), 0, REL - 1).astype(jnp.int32)
    span_ids = touch_ends(jax.random.randint(key_of[5], (N_BLK * N_SHARD,), 0, ROWS_OWN // NEG), jax.random.fold_in(key_of[5], 1), 0, (ROWS_OWN // NEG) - 1).astype(jnp.int32)
    return dict(table=table, relation=relation, owners=owners, rows=rows, rel_ids=rel_ids, span_ids=span_ids)


def edge_terms(source, target, rel_rows, spans, weight):
    half = source.shape[1] // 2
    s_re, s_im = source[:, :half], source[:, half:]
    r_re, r_im = rel_rows[:, :half], rel_rows[:, half:]
    query = jnp.concatenate([s_re * r_re - s_im * r_im, s_re * r_im + s_im * r_re], axis=1)
    pos_score = jnp.sum(query * target, axis=1)
    pos_grad = jax.nn.sigmoid(pos_score) - 1.0
    query_bf = lax.optimization_barrier(query.astype(jnp.bfloat16)).astype(jnp.float32)
    neg_score = jnp.einsum("ed,cnd->cen", query_bf, spans)
    neg_grad = lax.optimization_barrier((weight * jax.nn.sigmoid(neg_score)).astype(jnp.bfloat16)).astype(jnp.float32)
    query_grad = pos_grad[:, None] * target + jnp.einsum("cen,cnd->ed", neg_grad, spans)
    q_re, q_im = query_grad[:, :half], query_grad[:, half:]
    source_grad = jnp.concatenate([q_re * r_re + q_im * r_im, q_im * r_re - q_re * r_im], axis=1)
    rel_term = jnp.concatenate([q_re * s_re + q_im * s_im, q_im * s_re - q_re * s_im], axis=1)
    target_grad = pos_grad[:, None] * query
    span_term = jnp.einsum("cen,ed->cnd", neg_grad, query_bf)
    return source_grad, target_grad, rel_term, span_term


def reference(table, relation, owners, rows, rel_ids, span_ids):
    devices = N_BLK * N_SHARD
    edge_index = jnp.arange(EDGES, dtype=jnp.int32)
    blk_of = (edge_index // E_DEV) // N_SHARD
    ids = ((blk_of[:, None] * N_SHARD + owners) * ROWS_OWN + rows).astype(jnp.int32)
    starts = (jnp.arange(devices, dtype=jnp.int32) * ROWS_OWN + span_ids * NEG).astype(jnp.int32)
    weight = 1.0 / (float(N_BLK * NEG) ** 0.5)
    peer_table = (jnp.arange(N_BLK, dtype=jnp.int32)[None, :] * N_SHARD
                  + (jnp.arange(devices, dtype=jnp.int32) % N_SHARD)[:, None]).astype(jnp.int32)

    def one_device(device):
        first = (device * E_DEV).astype(jnp.int32)
        own_ids = lax.dynamic_slice(ids, (first, jnp.int32(0)), (E_DEV, 2))
        source = table[own_ids[:, 0]].astype(jnp.float32)
        target = table[own_ids[:, 1]].astype(jnp.float32)
        rel_rows = relation[lax.dynamic_slice(rel_ids, (first,), (E_DEV,))].astype(jnp.float32)
        peer_starts = starts[peer_table[device]]
        spans = jax.vmap(lambda begin: lax.dynamic_slice_in_dim(table, begin, NEG, 0))(peer_starts).astype(jnp.float32)
        return edge_terms(source, target, rel_rows, spans, weight)

    source_grad, target_grad, rel_term, span_term = lax.map(one_device, jnp.arange(devices, dtype=jnp.int32))
    entity_grad = jnp.zeros((ENT, D), jnp.float32)
    entity_grad = entity_grad.at[ids[:, 0]].add(source_grad.reshape(EDGES, D))
    entity_grad = entity_grad.at[ids[:, 1]].add(target_grad.reshape(EDGES, D))
    span_rows = (starts[peer_table][:, :, None] + jnp.arange(NEG, dtype=jnp.int32)[None, None, :]).astype(jnp.int32)
    entity_grad = entity_grad.at[span_rows.reshape(-1)].add(span_term.reshape(-1, D))
    relation_grad = jnp.zeros((REL, D), jnp.float32).at[rel_ids].add(rel_term.reshape(EDGES, D))
    return entity_grad, relation_grad
```

```python
import math

import jax
import jax.numpy as jnp
from jax import lax
from jax.sharding import PartitionSpec as P

NEG = 1024


def spread(value, axis, n):
    copies = jnp.broadcast_to(value[None], (n,) + value.shape)
    return lax.all_to_all(copies, axis, 0, 0, tiled=False)


def owner_rank(flat_owner, n_shard):
    count = flat_owner.shape[0]
    onehot = flat_owner[:, None] == jnp.arange(n_shard, dtype=jnp.int32)[None, :]
    index = jnp.arange(count, dtype=jnp.int32)
    earlier = (index[:, None] > index[None, :]).astype(jnp.bfloat16)
    before = jnp.dot(earlier, onehot.astype(jnp.bfloat16), preferred_element_type=jnp.float32)
    return jnp.sum(jnp.where(onehot, before, 0.0), axis=1).astype(jnp.int32)


def reduce_relation(local_relation):
    return lax.psum(local_relation, ("blk", "shard"))


def shards(table, relation, owners, rows, rel_ids, span_ids):
    n_shard = lax.axis_size("shard")
    n_blk = lax.axis_size("blk")
    edges = owners.shape[0]
    rows_own = table.shape[0]
    width = table.shape[1]
    half = width // 2
    capacity = 4 * edges // n_shard
    negatives = NEG
    span_start = span_ids[0] * negatives
    span = lax.dynamic_slice_in_dim(table, span_start, negatives, 0)
    spans = spread(span, "blk", n_blk).reshape(n_blk * negatives, width)
    flat_owner = owners.reshape(-1)
    flat_row = rows.reshape(-1)
    ranking = owner_rank(flat_owner, n_shard)
    slots = flat_owner * capacity + ranking
    requests = (
        jnp.zeros((n_shard * capacity,), jnp.int32)
        .at[slots]
        .set(flat_row)
        .reshape(n_shard, capacity)
    )
    asked_rows = lax.all_to_all(requests, "shard", split_axis=0, concat_axis=0, tiled=True)
    fetched = lax.all_to_all(table[asked_rows], "shard", split_axis=0, concat_axis=0, tiled=True)
    gotten = fetched.reshape(n_shard * capacity, width)[slots].reshape(edges, 2, width)
    source = gotten[:, 0].astype(jnp.float32)
    target = gotten[:, 1].astype(jnp.float32)
    rel_rows = relation[rel_ids].astype(jnp.float32)
    s_re, s_im = (source[:, :half], source[:, half:])
    r_re, r_im = (rel_rows[:, :half], rel_rows[:, half:])
    query = jnp.concatenate([s_re * r_re - s_im * r_im, s_re * r_im + s_im * r_re], axis=1)
    pos_grad = jax.nn.sigmoid(jnp.sum(query * target, axis=1)) - 1.0
    query_bf = query.astype(jnp.bfloat16)
    weight = 1.0 / math.sqrt(n_blk * negatives)
    neg_score = lax.dot_general(
        query_bf, spans, (((1,), (1,)), ((), ())), preferred_element_type=jnp.float32
    )
    neg_grad = (weight * jax.nn.sigmoid(neg_score)).astype(jnp.bfloat16)
    query_grad = pos_grad[:, None] * target + jnp.dot(
        neg_grad, spans, preferred_element_type=jnp.float32
    )
    span_part = lax.dot_general(
        neg_grad, query_bf, (((0,), (0,)), ((), ())), preferred_element_type=jnp.float32
    )
    carried = lax.all_to_all(
        span_part.reshape(n_blk, negatives, width), "blk", 0, 0, tiled=False
    ).sum(axis=0)
    q_re, q_im = (query_grad[:, :half], query_grad[:, half:])
    source_grad = jnp.concatenate([q_re * r_re + q_im * r_im, q_im * r_re - q_re * r_im], axis=1)
    rel_term = jnp.concatenate([q_re * s_re + q_im * s_im, q_im * s_re - q_re * s_im], axis=1)
    target_grad = pos_grad[:, None] * query
    local_relation = jnp.zeros((relation.shape[0], width), jnp.float32).at[rel_ids].add(rel_term)
    relation_grad = reduce_relation(local_relation)
    end_grads = jnp.stack([source_grad, target_grad], axis=1).reshape(2 * edges, width)
    outgoing = jnp.zeros((n_shard * capacity, width), jnp.float32).at[slots].set(end_grads)
    arrived = lax.all_to_all(
        outgoing.reshape(n_shard, capacity, width), "shard", split_axis=0, concat_axis=0, tiled=True
    )
    entity_grad = (
        jnp.zeros((rows_own, width), jnp.float32)
        .at[asked_rows.reshape(-1)]
        .add(arrived.reshape(-1, width))
    )
    current = lax.dynamic_slice_in_dim(entity_grad, span_start, negatives, 0)
    entity_grad = lax.dynamic_update_slice_in_dim(entity_grad, current + carried, span_start, 0)
    return (entity_grad, relation_grad)


def solution(mesh):
    in_specs = (
        P(("blk", "shard"), None),
        P(),
        P(("blk", "shard"), None),
        P(("blk", "shard"), None),
        P(("blk", "shard")),
        P(("blk", "shard")),
    )
    out_specs = (P(("blk", "shard"), None), P())
    return jax.shard_map(shards, mesh=mesh, in_specs=in_specs, out_specs=out_specs, check_vma=False)
```

```python
import math

import jax
import jax.numpy as jnp
from jax import lax
from jax.sharding import PartitionSpec as P

NEG = 1024


def spread(value, axis, n):
    copies = jnp.broadcast_to(value[None], (n,) + value.shape)
    return lax.all_to_all(copies, axis, 0, 0, tiled=False)


def owner_rank(flat_owner, n_shard):
    count = flat_owner.shape[0]
    onehot = flat_owner[:, None] == jnp.arange(n_shard, dtype=jnp.int32)[None, :]
    index = jnp.arange(count, dtype=jnp.int32)
    earlier = (index[:, None] > index[None, :]).astype(jnp.bfloat16)
    before = jnp.dot(earlier, onehot.astype(jnp.bfloat16), preferred_element_type=jnp.float32)
    return jnp.sum(jnp.where(onehot, before, 0.0), axis=1).astype(jnp.int32)


def reduce_relation(local_relation, n_blk, n_shard):
    rows, width = local_relation.shape
    total = rows * width
    lane = 128
    per_peer = -(-total // (n_blk * n_shard * lane)) * lane
    piece = n_shard * per_peer
    flat = jnp.pad(local_relation.reshape(-1), (0, n_blk * piece - total))
    parts = flat.reshape(n_blk, 8, piece // 8)
    mine = lax.all_to_all(parts, "blk", 0, 0, tiled=False).sum(axis=0)
    mine = mine.reshape(n_shard, per_peer)
    small = lax.all_to_all(mine, "shard", 0, 0, tiled=False).sum(axis=0)
    gathered = spread(small, "shard", n_shard).reshape(8, piece // 8)
    whole = spread(gathered, "blk", n_blk)
    return whole.reshape(-1)[:total].reshape(rows, width)


def shards(table, relation, owners, rows, rel_ids, span_ids):
    n_shard = lax.axis_size("shard")
    n_blk = lax.axis_size("blk")
    edges = owners.shape[0]
    rows_own = table.shape[0]
    width = table.shape[1]
    half = width // 2
    capacity = 4 * edges // n_shard
    negatives = NEG
    span_start = span_ids[0] * negatives
    span = lax.dynamic_slice_in_dim(table, span_start, negatives, 0)
    spans = spread(span, "blk", n_blk).reshape(n_blk * negatives, width)
    flat_owner = owners.reshape(-1)
    flat_row = rows.reshape(-1)
    ranking = owner_rank(flat_owner, n_shard)
    slots = flat_owner * capacity + ranking
    requests = (
        jnp.zeros((n_shard * capacity,), jnp.int32)
        .at[slots]
        .set(flat_row)
        .reshape(n_shard, capacity)
    )
    asked_rows = lax.all_to_all(requests, "shard", split_axis=0, concat_axis=0, tiled=True)
    fetched = lax.all_to_all(table[asked_rows], "shard", split_axis=0, concat_axis=0, tiled=True)
    gotten = fetched.reshape(n_shard * capacity, width)[slots].reshape(edges, 2, width)
    source = gotten[:, 0].astype(jnp.float32)
    target = gotten[:, 1].astype(jnp.float32)
    rel_rows = relation[rel_ids].astype(jnp.float32)
    s_re, s_im = (source[:, :half], source[:, half:])
    r_re, r_im = (rel_rows[:, :half], rel_rows[:, half:])
    query = jnp.concatenate([s_re * r_re - s_im * r_im, s_re * r_im + s_im * r_re], axis=1)
    pos_grad = jax.nn.sigmoid(jnp.sum(query * target, axis=1)) - 1.0
    query_bf = query.astype(jnp.bfloat16)
    weight = 1.0 / math.sqrt(n_blk * negatives)
    neg_score = lax.dot_general(
        query_bf, spans, (((1,), (1,)), ((), ())), preferred_element_type=jnp.float32
    )
    neg_grad = (weight * jax.nn.sigmoid(neg_score)).astype(jnp.bfloat16)
    query_grad = pos_grad[:, None] * target + jnp.dot(
        neg_grad, spans, preferred_element_type=jnp.float32
    )
    span_part = lax.dot_general(
        neg_grad, query_bf, (((0,), (0,)), ((), ())), preferred_element_type=jnp.float32
    )
    carried = lax.all_to_all(
        span_part.reshape(n_blk, negatives, width), "blk", 0, 0, tiled=False
    ).sum(axis=0)
    q_re, q_im = (query_grad[:, :half], query_grad[:, half:])
    source_grad = jnp.concatenate([q_re * r_re + q_im * r_im, q_im * r_re - q_re * r_im], axis=1)
    rel_term = jnp.concatenate([q_re * s_re + q_im * s_im, q_im * s_re - q_re * s_im], axis=1)
    target_grad = pos_grad[:, None] * query
    local_relation = jnp.zeros((relation.shape[0], width), jnp.float32).at[rel_ids].add(rel_term)
    relation_grad = reduce_relation(local_relation, n_blk, n_shard)
    end_grads = jnp.stack([source_grad, target_grad], axis=1).reshape(2 * edges, width)
    outgoing = jnp.zeros((n_shard * capacity, width), jnp.float32).at[slots].set(end_grads)
    arrived = lax.all_to_all(
        outgoing.reshape(n_shard, capacity, width), "shard", split_axis=0, concat_axis=0, tiled=True
    )
    entity_grad = (
        jnp.zeros((rows_own, width), jnp.float32)
        .at[asked_rows.reshape(-1)]
        .add(arrived.reshape(-1, width))
    )
    current = lax.dynamic_slice_in_dim(entity_grad, span_start, negatives, 0)
    entity_grad = lax.dynamic_update_slice_in_dim(entity_grad, current + carried, span_start, 0)
    return (entity_grad, relation_grad)


def solution(mesh):
    in_specs = (
        P(("blk", "shard"), None),
        P(),
        P(("blk", "shard"), None),
        P(("blk", "shard"), None),
        P(("blk", "shard")),
        P(("blk", "shard")),
    )
    out_specs = (P(("blk", "shard"), None), P())
    return jax.shard_map(shards, mesh=mesh, in_specs=in_specs, out_specs=out_specs, check_vma=False)
```

```python
import math

import jax
import jax.numpy as jnp
from jax import lax
from jax.sharding import PartitionSpec as P

NEG = 1024
LANE = 128


def shifted(value, axis, n, by):
    return lax.ppermute(value, axis, [(i, (i + by) % n) for i in range(n)])


def spread(value, axis, n):
    copies = jnp.broadcast_to(value[None], (n,) + value.shape)
    return lax.all_to_all(copies, axis, 0, 0, tiled=False)


def owner_rank(flat_owner, n_shard):
    count = flat_owner.shape[0]
    onehot = flat_owner[:, None] == jnp.arange(n_shard, dtype=jnp.int32)[None, :]
    index = jnp.arange(count, dtype=jnp.int32)
    earlier = (index[:, None] > index[None, :]).astype(jnp.bfloat16)
    before = jnp.dot(earlier, onehot.astype(jnp.bfloat16), preferred_element_type=jnp.float32)
    return jnp.sum(jnp.where(onehot, before, 0.0), axis=1).astype(jnp.int32)


def shards(table, relation, owners, rows, rel_ids, span_ids):
    n_shard = lax.axis_size("shard")
    n_blk = lax.axis_size("blk")
    me_blk = lax.axis_index("blk")
    edges = owners.shape[0]
    rows_own = table.shape[0]
    width = table.shape[1]
    half = width // 2
    capacity = 4 * edges // n_shard
    negatives = NEG
    span_start = span_ids[0] * negatives
    span = lax.dynamic_slice_in_dim(table, span_start, negatives, 0)
    spans = jnp.concatenate(
        [span] + [shifted(span, "blk", n_blk, d) for d in range(1, n_blk)], axis=0
    )
    flat_owner = owners.reshape(-1)
    flat_row = rows.reshape(-1)
    ranking = owner_rank(flat_owner, n_shard)
    slots = flat_owner * capacity + ranking
    requests = (
        jnp.zeros((n_shard * capacity,), jnp.int32)
        .at[slots]
        .set(flat_row)
        .reshape(n_shard, capacity)
    )
    asked_rows = lax.all_to_all(requests, "shard", split_axis=0, concat_axis=0, tiled=True)
    fetched = lax.all_to_all(table[asked_rows], "shard", split_axis=0, concat_axis=0, tiled=True)
    gotten = fetched.reshape(n_shard * capacity, width)[slots].reshape(edges, 2, width)
    source = gotten[:, 0].astype(jnp.float32)
    target = gotten[:, 1].astype(jnp.float32)
    rel_rows = relation[rel_ids].astype(jnp.float32)
    s_re, s_im = (source[:, :half], source[:, half:])
    r_re, r_im = (rel_rows[:, :half], rel_rows[:, half:])
    query = jnp.concatenate([s_re * r_re - s_im * r_im, s_re * r_im + s_im * r_re], axis=1)
    pos_grad = jax.nn.sigmoid(jnp.sum(query * target, axis=1)) - 1.0
    query_bf = query.astype(jnp.bfloat16)
    weight = 1.0 / math.sqrt(n_blk * negatives)
    neg_score = lax.dot_general(
        query_bf, spans, (((1,), (1,)), ((), ())), preferred_element_type=jnp.float32
    )
    neg_grad = (weight * jax.nn.sigmoid(neg_score)).astype(jnp.bfloat16)
    query_grad = pos_grad[:, None] * target + jnp.dot(
        neg_grad, spans, preferred_element_type=jnp.float32
    )
    span_part = lax.dot_general(
        neg_grad, query_bf, (((0,), (0,)), ((), ())), preferred_element_type=jnp.float32
    ).reshape(n_blk, negatives, width)
    carried = span_part[0]
    for d in range(1, n_blk):
        carried = carried + shifted(span_part[d], "blk", n_blk, -d)
    q_re, q_im = (query_grad[:, :half], query_grad[:, half:])
    source_grad = jnp.concatenate([q_re * r_re + q_im * r_im, q_im * r_re - q_re * r_im], axis=1)
    rel_term = jnp.concatenate([q_re * s_re + q_im * s_im, q_im * s_re - q_re * s_im], axis=1)
    target_grad = pos_grad[:, None] * query

    rel_rows_n = relation.shape[0]
    total = rel_rows_n * width
    per_peer = -(-total // (n_blk * n_shard * LANE)) * LANE
    local_relation = jnp.zeros((rel_rows_n, width), jnp.float32).at[rel_ids].add(rel_term)
    quarters = jnp.pad(local_relation.reshape(-1), (0, n_blk * n_shard * per_peer - total))
    quarters = quarters.reshape(n_blk, n_shard, per_peer)
    mine = lax.dynamic_index_in_dim(quarters, me_blk, 0, keepdims=False)
    for d in range(1, n_blk):
        outgoing_quarter = lax.dynamic_index_in_dim(quarters, (me_blk + d) % n_blk, 0, keepdims=False)
        mine = mine + shifted(outgoing_quarter, "blk", n_blk, d)

    sub = 8
    grad_lanes = capacity * width // sub
    rel_lanes = -(-per_peer // (sub * LANE)) * LANE
    end_grads = jnp.stack([source_grad, target_grad], axis=1).reshape(2 * edges, width)
    outgoing = jnp.zeros((n_shard * capacity, width), jnp.float32).at[slots].set(end_grads)
    rel_out = jnp.pad(mine, ((0, 0), (0, sub * rel_lanes - per_peer))).reshape(n_shard, sub, rel_lanes)
    payload = jnp.concatenate([outgoing.reshape(n_shard, sub, grad_lanes), rel_out], axis=2)
    arrived = lax.all_to_all(payload, "shard", split_axis=0, concat_axis=0, tiled=True)
    arrived_grads = arrived[:, :, :grad_lanes].reshape(n_shard * capacity, width)
    piece = arrived[:, :, grad_lanes:].reshape(n_shard, sub * rel_lanes)[:, :per_peer].sum(axis=0)

    quarter = spread(piece, "shard", n_shard)
    held = jnp.stack([quarter] + [shifted(quarter, "blk", n_blk, d) for d in range(1, n_blk)])
    order = (me_blk - jnp.arange(n_blk, dtype=jnp.int32)) % n_blk
    relation_grad = jnp.take(held, order, axis=0).reshape(-1)[:total].reshape(rel_rows_n, width)

    entity_grad = (
        jnp.zeros((rows_own, width), jnp.float32)
        .at[asked_rows.reshape(-1)]
        .add(arrived_grads)
    )
    current = lax.dynamic_slice_in_dim(entity_grad, span_start, negatives, 0)
    entity_grad = lax.dynamic_update_slice_in_dim(entity_grad, current + carried, span_start, 0)
    return (entity_grad, relation_grad)


def solution(mesh):
    in_specs = (
        P(("blk", "shard"), None),
        P(),
        P(("blk", "shard"), None),
        P(("blk", "shard"), None),
        P(("blk", "shard")),
        P(("blk", "shard")),
    )
    out_specs = (P(("blk", "shard"), None), P())
    return jax.shard_map(shards, mesh=mesh, in_specs=in_specs, out_specs=out_specs, check_vma=False)
```

```python
import math

import jax
import jax.numpy as jnp
from jax import lax
from jax.sharding import PartitionSpec as P

NEG = 1024
LANE = 128


def shifted(value, axis, n, by):
    return lax.ppermute(value, axis, [(i, (i + by) % n) for i in range(n)])


def spread(value, axis, n):
    copies = jnp.broadcast_to(value[None], (n,) + value.shape)
    return lax.all_to_all(copies, axis, 0, 0, tiled=False)


def owner_rank(flat_owner, n_shard):
    count = flat_owner.shape[0]
    onehot = flat_owner[:, None] == jnp.arange(n_shard, dtype=jnp.int32)[None, :]
    index = jnp.arange(count, dtype=jnp.int32)
    earlier = (index[:, None] > index[None, :]).astype(jnp.bfloat16)
    before = jnp.dot(earlier, onehot.astype(jnp.bfloat16), preferred_element_type=jnp.float32)
    return jnp.sum(jnp.where(onehot, before, 0.0), axis=1).astype(jnp.int32)


def shards(table, relation, owners, rows, rel_ids, span_ids):
    n_shard = lax.axis_size("shard")
    n_blk = lax.axis_size("blk")
    me_blk = lax.axis_index("blk")
    edges = owners.shape[0]
    rows_own = table.shape[0]
    width = table.shape[1]
    half = width // 2
    capacity = 4 * edges // n_shard
    negatives = NEG
    span_start = span_ids[0] * negatives
    span = lax.dynamic_slice_in_dim(table, span_start, negatives, 0)
    spans = jnp.concatenate(
        [span] + [shifted(span, "blk", n_blk, d) for d in range(1, n_blk)], axis=0
    )
    flat_owner = owners.reshape(-1)
    flat_row = rows.reshape(-1)
    ranking = owner_rank(flat_owner, n_shard)
    slots = flat_owner * capacity + ranking
    requests = (
        jnp.zeros((n_shard * capacity,), jnp.int32)
        .at[slots]
        .set(flat_row)
        .reshape(n_shard, capacity)
    )
    asked_rows = lax.all_to_all(requests, "shard", split_axis=0, concat_axis=0, tiled=True)
    fetched = lax.all_to_all(table[asked_rows], "shard", split_axis=0, concat_axis=0, tiled=True)
    gotten = fetched.reshape(n_shard * capacity, width)[slots].reshape(edges, 2, width)
    source = gotten[:, 0].astype(jnp.float32)
    target = gotten[:, 1].astype(jnp.float32)
    rel_rows = relation[rel_ids].astype(jnp.float32)
    s_re, s_im = (source[:, :half], source[:, half:])
    r_re, r_im = (rel_rows[:, :half], rel_rows[:, half:])
    query = jnp.concatenate([s_re * r_re - s_im * r_im, s_re * r_im + s_im * r_re], axis=1)
    pos_grad = jax.nn.sigmoid(jnp.sum(query * target, axis=1)) - 1.0
    query_bf = query.astype(jnp.bfloat16)
    weight = 1.0 / math.sqrt(n_blk * negatives)
    neg_score = lax.dot_general(
        query_bf, spans, (((1,), (1,)), ((), ())), preferred_element_type=jnp.float32
    )
    neg_grad = (weight * jax.nn.sigmoid(neg_score)).astype(jnp.bfloat16)
    query_grad = pos_grad[:, None] * target + jnp.dot(
        neg_grad, spans, preferred_element_type=jnp.float32
    )
    span_part = lax.dot_general(
        neg_grad, query_bf, (((0,), (0,)), ((), ())), preferred_element_type=jnp.float32
    ).reshape(n_blk, negatives, width)
    carried = span_part[0]
    for d in range(1, n_blk):
        carried = carried + shifted(span_part[d], "blk", n_blk, -d)
    q_re, q_im = (query_grad[:, :half], query_grad[:, half:])
    source_grad = jnp.concatenate([q_re * r_re + q_im * r_im, q_im * r_re - q_re * r_im], axis=1)
    rel_term = jnp.concatenate([q_re * s_re + q_im * s_im, q_im * s_re - q_re * s_im], axis=1)
    target_grad = pos_grad[:, None] * query

    rel_rows_n = relation.shape[0]
    chunk = -(-rel_rows_n // (n_blk * n_shard))
    quarter_rows = n_shard * chunk
    local_relation = (
        jnp.zeros((n_blk * quarter_rows, width), jnp.float32).at[rel_ids].add(rel_term)
    )
    quarters = local_relation.reshape(n_blk, quarter_rows, width)
    mine = lax.dynamic_index_in_dim(quarters, me_blk, 0, keepdims=False)
    for d in range(1, n_blk):
        outgoing_quarter = lax.dynamic_index_in_dim(quarters, (me_blk + d) % n_blk, 0, keepdims=False)
        mine = mine + shifted(outgoing_quarter, "blk", n_blk, d)

    end_grads = jnp.stack([source_grad, target_grad], axis=1).reshape(2 * edges, width)
    outgoing = jnp.zeros((n_shard * capacity, width), jnp.float32).at[slots].set(end_grads)
    payload = jnp.concatenate(
        [outgoing.reshape(n_shard, capacity, width), mine.reshape(n_shard, chunk, width)], axis=1
    )
    arrived = lax.all_to_all(payload, "shard", split_axis=0, concat_axis=0, tiled=True)
    arrived_grads = arrived[:, :capacity].reshape(n_shard * capacity, width)
    piece = arrived[:, capacity:].sum(axis=0)

    quarter = spread(piece, "shard", n_shard).reshape(quarter_rows, width)
    held = jnp.stack([quarter] + [shifted(quarter, "blk", n_blk, d) for d in range(1, n_blk)])
    order = (me_blk - jnp.arange(n_blk, dtype=jnp.int32)) % n_blk
    relation_grad = jnp.take(held, order, axis=0).reshape(n_blk * quarter_rows, width)[:rel_rows_n]

    entity_grad = (
        jnp.zeros((rows_own, width), jnp.float32)
        .at[asked_rows.reshape(-1)]
        .add(arrived_grads)
    )
    current = lax.dynamic_slice_in_dim(entity_grad, span_start, negatives, 0)
    entity_grad = lax.dynamic_update_slice_in_dim(entity_grad, current + carried, span_start, 0)
    return (entity_grad, relation_grad)


def solution(mesh):
    in_specs = (
        P(("blk", "shard"), None),
        P(),
        P(("blk", "shard"), None),
        P(("blk", "shard"), None),
        P(("blk", "shard")),
        P(("blk", "shard")),
    )
    out_specs = (P(("blk", "shard"), None), P())
    return jax.shard_map(shards, mesh=mesh, in_specs=in_specs, out_specs=out_specs, check_vma=False)
```

```python
import math

import jax
import jax.numpy as jnp
from jax import lax
from jax.sharding import PartitionSpec as P

NEG = 1024
LANE = 128


def shifted(value, axis, n, by):
    return lax.ppermute(value, axis, [(i, (i + by) % n) for i in range(n)])


def spread(value, axis, n):
    copies = jnp.broadcast_to(value[None], (n,) + value.shape)
    return lax.all_to_all(copies, axis, 0, 0, tiled=False)


SHARD_DIMS = (4, 8, 2)


def shard_moves(sizes, dim, by):
    n = sizes[0] * sizes[1] * sizes[2]
    pairs = []
    for s in range(n):
        coords = [s // (sizes[1] * sizes[2]), (s // sizes[2]) % sizes[1], s % sizes[2]]
        coords[dim] = (coords[dim] + by) % sizes[dim]
        pairs.append((s, (coords[0] * sizes[1] + coords[1]) * sizes[2] + coords[2]))
    return pairs


def reduce_over_shard(block, n_shard, width):
    sizes = SHARD_DIMS
    me = lax.axis_index("shard")
    mine_at = [me // (sizes[1] * sizes[2]), (me // sizes[2]) % sizes[1], me % sizes[2]]
    levels = (2, 0, 1)
    for dim in levels:
        n = sizes[dim]
        parts = block.reshape(n, -1, width)
        block = lax.dynamic_index_in_dim(parts, mine_at[dim], 0, keepdims=False)
        for d in range(1, n):
            going = lax.dynamic_index_in_dim(parts, (mine_at[dim] + d) % n, 0, keepdims=False)
            block = block + lax.ppermute(going, "shard", shard_moves(sizes, dim, d))
    for dim in reversed(levels):
        n = sizes[dim]
        held = [block] + [lax.ppermute(block, "shard", shard_moves(sizes, dim, d)) for d in range(1, n)]
        order = (mine_at[dim] - jnp.arange(n, dtype=jnp.int32)) % n
        block = jnp.take(jnp.stack(held), order, axis=0).reshape(-1, width)
    return block


def owner_rank(flat_owner, n_shard):
    count = flat_owner.shape[0]
    onehot = flat_owner[:, None] == jnp.arange(n_shard, dtype=jnp.int32)[None, :]
    index = jnp.arange(count, dtype=jnp.int32)
    earlier = (index[:, None] > index[None, :]).astype(jnp.bfloat16)
    before = jnp.dot(earlier, onehot.astype(jnp.bfloat16), preferred_element_type=jnp.float32)
    return jnp.sum(jnp.where(onehot, before, 0.0), axis=1).astype(jnp.int32)


def shards(table, relation, owners, rows, rel_ids, span_ids):
    n_shard = lax.axis_size("shard")
    n_blk = lax.axis_size("blk")
    me_blk = lax.axis_index("blk")
    edges = owners.shape[0]
    rows_own = table.shape[0]
    width = table.shape[1]
    half = width // 2
    capacity = 4 * edges // n_shard
    negatives = NEG
    span_start = span_ids[0] * negatives
    span = lax.dynamic_slice_in_dim(table, span_start, negatives, 0)
    spans = jnp.concatenate(
        [span] + [shifted(span, "blk", n_blk, d) for d in range(1, n_blk)], axis=0
    )
    flat_owner = owners.reshape(-1)
    flat_row = rows.reshape(-1)
    ranking = owner_rank(flat_owner, n_shard)
    slots = flat_owner * capacity + ranking
    requests = (
        jnp.zeros((n_shard * capacity,), jnp.int32)
        .at[slots]
        .set(flat_row)
        .reshape(n_shard, capacity)
    )
    asked_rows = lax.all_to_all(requests, "shard", split_axis=0, concat_axis=0, tiled=True)
    fetch_rows = capacity * width // LANE
    sending = table[asked_rows].reshape(n_shard, fetch_rows, LANE)
    fetched = lax.all_to_all(sending, "shard", split_axis=0, concat_axis=0, tiled=True)
    gotten = fetched.reshape(n_shard * capacity, width)[slots].reshape(edges, 2, width)
    source = gotten[:, 0].astype(jnp.float32)
    target = gotten[:, 1].astype(jnp.float32)
    rel_rows = relation[rel_ids].astype(jnp.float32)
    s_re, s_im = (source[:, :half], source[:, half:])
    r_re, r_im = (rel_rows[:, :half], rel_rows[:, half:])
    query = jnp.concatenate([s_re * r_re - s_im * r_im, s_re * r_im + s_im * r_re], axis=1)
    pos_grad = jax.nn.sigmoid(jnp.sum(query * target, axis=1)) - 1.0
    query_bf = query.astype(jnp.bfloat16)
    weight = 1.0 / math.sqrt(n_blk * negatives)
    neg_score = lax.dot_general(
        query_bf, spans, (((1,), (1,)), ((), ())), preferred_element_type=jnp.float32
    )
    neg_grad = (weight * jax.nn.sigmoid(neg_score)).astype(jnp.bfloat16)
    query_grad = pos_grad[:, None] * target + jnp.dot(
        neg_grad, spans, preferred_element_type=jnp.float32
    )
    span_part = lax.dot_general(
        neg_grad, query_bf, (((0,), (0,)), ((), ())), preferred_element_type=jnp.float32
    ).reshape(n_blk, negatives, width)
    carried = span_part[0]
    for d in range(1, n_blk):
        carried = carried + shifted(span_part[d], "blk", n_blk, -d)
    q_re, q_im = (query_grad[:, :half], query_grad[:, half:])
    source_grad = jnp.concatenate([q_re * r_re + q_im * r_im, q_im * r_re - q_re * r_im], axis=1)
    rel_term = jnp.concatenate([q_re * s_re + q_im * s_im, q_im * s_re - q_re * s_im], axis=1)
    target_grad = pos_grad[:, None] * query

    rel_rows_n = relation.shape[0]
    chunk = -(-rel_rows_n // (n_blk * n_shard))
    quarter_rows = n_shard * chunk
    local_relation = (
        jnp.zeros((n_blk * quarter_rows, width), jnp.float32).at[rel_ids].add(rel_term)
    )
    quarters = local_relation.reshape(n_blk, quarter_rows, width)
    mine = lax.dynamic_index_in_dim(quarters, me_blk, 0, keepdims=False)
    for d in range(1, n_blk):
        outgoing_quarter = lax.dynamic_index_in_dim(quarters, (me_blk + d) % n_blk, 0, keepdims=False)
        mine = mine + shifted(outgoing_quarter, "blk", n_blk, d)
    relation_grad = reduce_over_shard(mine, n_shard, width)
    held = jnp.stack([relation_grad] + [shifted(relation_grad, "blk", n_blk, d) for d in range(1, n_blk)])
    order = (me_blk - jnp.arange(n_blk, dtype=jnp.int32)) % n_blk
    relation_grad = jnp.take(held, order, axis=0).reshape(n_blk * quarter_rows, width)[:rel_rows_n]

    sub = 8
    grad_lanes = capacity * width // sub
    end_grads = jnp.stack([source_grad, target_grad], axis=1).reshape(2 * edges, width)
    outgoing = jnp.zeros((n_shard * capacity, width), jnp.float32).at[slots].set(end_grads)
    payload = outgoing.reshape(n_shard, sub, grad_lanes)
    arrived = lax.all_to_all(payload, "shard", split_axis=0, concat_axis=0, tiled=True)
    arrived_grads = arrived.reshape(n_shard * capacity, width)

    entity_grad = (
        jnp.zeros((rows_own, width), jnp.float32)
        .at[asked_rows.reshape(-1)]
        .add(arrived_grads)
    )
    current = lax.dynamic_slice_in_dim(entity_grad, span_start, negatives, 0)
    entity_grad = lax.dynamic_update_slice_in_dim(entity_grad, current + carried, span_start, 0)
    return (entity_grad, relation_grad)


def solution(mesh):
    in_specs = (
        P(("blk", "shard"), None),
        P(),
        P(("blk", "shard"), None),
        P(("blk", "shard"), None),
        P(("blk", "shard")),
        P(("blk", "shard")),
    )
    out_specs = (P(("blk", "shard"), None), P())
    return jax.shard_map(shards, mesh=mesh, in_specs=in_specs, out_specs=out_specs, check_vma=False)
```

```python
import math

import jax
import jax.numpy as jnp
from jax import lax
from jax.sharding import PartitionSpec as P

NEG = 1024
LANE = 128


def shifted(value, axis, n, by):
    return lax.ppermute(value, axis, [(i, (i + by) % n) for i in range(n)])


def spread(value, axis, n):
    copies = jnp.broadcast_to(value[None], (n,) + value.shape)
    return lax.all_to_all(copies, axis, 0, 0, tiled=False)


def owner_rank(flat_owner, n_shard):
    count = flat_owner.shape[0]
    onehot = flat_owner[:, None] == jnp.arange(n_shard, dtype=jnp.int32)[None, :]
    index = jnp.arange(count, dtype=jnp.int32)
    earlier = (index[:, None] > index[None, :]).astype(jnp.bfloat16)
    before = jnp.dot(earlier, onehot.astype(jnp.bfloat16), preferred_element_type=jnp.float32)
    return jnp.sum(jnp.where(onehot, before, 0.0), axis=1).astype(jnp.int32)


def shards(table, relation, owners, rows, rel_ids, span_ids):
    n_shard = lax.axis_size("shard")
    n_blk = lax.axis_size("blk")
    me_blk = lax.axis_index("blk")
    edges = owners.shape[0]
    rows_own = table.shape[0]
    width = table.shape[1]
    half = width // 2
    capacity = 4 * edges // n_shard
    negatives = NEG
    span_start = span_ids[0] * negatives
    span = lax.dynamic_slice_in_dim(table, span_start, negatives, 0)
    spans = jnp.concatenate(
        [span] + [shifted(span, "blk", n_blk, d) for d in range(1, n_blk)], axis=0
    )
    flat_owner = owners.reshape(-1)
    flat_row = rows.reshape(-1)
    ranking = owner_rank(flat_owner, n_shard)
    slots = flat_owner * capacity + ranking
    requests = (
        jnp.zeros((n_shard * capacity,), jnp.int32)
        .at[slots]
        .set(flat_row)
        .reshape(n_shard, capacity)
    )
    asked_rows = lax.all_to_all(requests, "shard", split_axis=0, concat_axis=0, tiled=True)
    fetched = lax.all_to_all(table[asked_rows], "shard", split_axis=0, concat_axis=0, tiled=True)
    gotten = fetched.reshape(n_shard * capacity, width)[slots].reshape(edges, 2, width)
    source = gotten[:, 0].astype(jnp.float32)
    target = gotten[:, 1].astype(jnp.float32)
    rel_rows = relation[rel_ids].astype(jnp.float32)
    s_re, s_im = (source[:, :half], source[:, half:])
    r_re, r_im = (rel_rows[:, :half], rel_rows[:, half:])
    query = jnp.concatenate([s_re * r_re - s_im * r_im, s_re * r_im + s_im * r_re], axis=1)
    pos_grad = jax.nn.sigmoid(jnp.sum(query * target, axis=1)) - 1.0
    query_bf = query.astype(jnp.bfloat16)
    weight = 1.0 / math.sqrt(n_blk * negatives)
    neg_score = lax.dot_general(
        query_bf, spans, (((1,), (1,)), ((), ())), preferred_element_type=jnp.float32
    )
    neg_grad = (weight * jax.nn.sigmoid(neg_score)).astype(jnp.bfloat16)
    query_grad = pos_grad[:, None] * target + jnp.dot(
        neg_grad, spans, preferred_element_type=jnp.float32
    )
    span_part = lax.dot_general(
        neg_grad, query_bf, (((0,), (0,)), ((), ())), preferred_element_type=jnp.float32
    ).reshape(n_blk, negatives, width)
    carried = span_part[0]
    for d in range(1, n_blk):
        carried = carried + shifted(span_part[d], "blk", n_blk, -d)
    q_re, q_im = (query_grad[:, :half], query_grad[:, half:])
    source_grad = jnp.concatenate([q_re * r_re + q_im * r_im, q_im * r_re - q_re * r_im], axis=1)
    rel_term = jnp.concatenate([q_re * s_re + q_im * s_im, q_im * s_re - q_re * s_im], axis=1)
    target_grad = pos_grad[:, None] * query

    rel_rows_n = relation.shape[0]
    total = rel_rows_n * width
    per_peer = -(-total // (n_blk * n_shard * LANE)) * LANE
    local_relation = jnp.zeros((rel_rows_n, width), jnp.float32).at[rel_ids].add(rel_term)
    quarters = jnp.pad(local_relation.reshape(-1), (0, n_blk * n_shard * per_peer - total))
    quarters = quarters.reshape(n_blk, n_shard, per_peer)
    mine = lax.dynamic_index_in_dim(quarters, me_blk, 0, keepdims=False)
    for d in range(1, n_blk):
        outgoing_quarter = lax.dynamic_index_in_dim(quarters, (me_blk + d) % n_blk, 0, keepdims=False)
        mine = mine + shifted(outgoing_quarter, "blk", n_blk, d)

    small = lax.all_to_all(mine, "shard", 0, 0, tiled=False).sum(axis=0)
    quarter = spread(small, "shard", n_shard)
    held = jnp.stack([quarter] + [shifted(quarter, "blk", n_blk, d) for d in range(1, n_blk)])
    order = (me_blk - jnp.arange(n_blk, dtype=jnp.int32)) % n_blk
    relation_grad = jnp.take(held, order, axis=0).reshape(-1)[:total].reshape(rel_rows_n, width)

    sub = 8
    grad_lanes = capacity * width // sub
    end_grads = jnp.stack([source_grad, target_grad], axis=1).reshape(2 * edges, width)
    outgoing = jnp.zeros((n_shard * capacity, width), jnp.float32).at[slots].set(end_grads)
    payload = outgoing.reshape(n_shard, sub, grad_lanes)
    arrived = lax.all_to_all(payload, "shard", split_axis=0, concat_axis=0, tiled=True)
    arrived_grads = arrived.reshape(n_shard * capacity, width)

    entity_grad = (
        jnp.zeros((rows_own, width), jnp.float32)
        .at[asked_rows.reshape(-1)]
        .add(arrived_grads)
    )
    current = lax.dynamic_slice_in_dim(entity_grad, span_start, negatives, 0)
    entity_grad = lax.dynamic_update_slice_in_dim(entity_grad, current + carried, span_start, 0)
    return (entity_grad, relation_grad)


def solution(mesh):
    in_specs = (
        P(("blk", "shard"), None),
        P(),
        P(("blk", "shard"), None),
        P(("blk", "shard"), None),
        P(("blk", "shard")),
        P(("blk", "shard")),
    )
    out_specs = (P(("blk", "shard"), None), P())
    return jax.shard_map(shards, mesh=mesh, in_specs=in_specs, out_specs=out_specs, check_vma=False)
```

```python
import math

import jax
import jax.numpy as jnp
from jax import lax
from jax.sharding import PartitionSpec as P

NEG = 1024
LANE = 128


def shifted(value, axis, n, by):
    return lax.ppermute(value, axis, [(i, (i + by) % n) for i in range(n)])


def spread(value, axis, n):
    copies = jnp.broadcast_to(value[None], (n,) + value.shape)
    return lax.all_to_all(copies, axis, 0, 0, tiled=False)


def owner_rank(flat_owner, n_shard):
    count = flat_owner.shape[0]
    onehot = flat_owner[:, None] == jnp.arange(n_shard, dtype=jnp.int32)[None, :]
    index = jnp.arange(count, dtype=jnp.int32)
    earlier = (index[:, None] > index[None, :]).astype(jnp.bfloat16)
    before = jnp.dot(earlier, onehot.astype(jnp.bfloat16), preferred_element_type=jnp.float32)
    return jnp.sum(jnp.where(onehot, before, 0.0), axis=1).astype(jnp.int32)


def shards(table, relation, owners, rows, rel_ids, span_ids):
    n_shard = lax.axis_size("shard")
    n_blk = lax.axis_size("blk")
    me_blk = lax.axis_index("blk")
    edges = owners.shape[0]
    rows_own = table.shape[0]
    width = table.shape[1]
    half = width // 2
    capacity = 4 * edges // n_shard
    negatives = NEG
    span_start = span_ids[0] * negatives
    span = lax.dynamic_slice_in_dim(table, span_start, negatives, 0)
    spans = jnp.concatenate(
        [span] + [shifted(span, "blk", n_blk, d) for d in range(1, n_blk)], axis=0
    )
    flat_owner = owners.reshape(-1)
    flat_row = rows.reshape(-1)
    ranking = owner_rank(flat_owner, n_shard)
    slots = flat_owner * capacity + ranking
    requests = (
        jnp.zeros((n_shard * capacity,), jnp.int32)
        .at[slots]
        .set(flat_row)
        .reshape(n_shard, capacity)
    )
    asked_rows = lax.all_to_all(requests, "shard", split_axis=0, concat_axis=0, tiled=True)
    fetched = lax.all_to_all(table[asked_rows], "shard", split_axis=0, concat_axis=0, tiled=True)
    fetched = fetched.reshape(n_shard * capacity, width)
    end_slots = slots.reshape(edges, 2)
    source_slots = end_slots[:, 0]
    target_slots = end_slots[:, 1]
    source = fetched[source_slots].astype(jnp.float32)
    target = fetched[target_slots].astype(jnp.float32)
    rel_rows = relation[rel_ids].astype(jnp.float32)
    s_re, s_im = (source[:, :half], source[:, half:])
    r_re, r_im = (rel_rows[:, :half], rel_rows[:, half:])
    query = jnp.concatenate([s_re * r_re - s_im * r_im, s_re * r_im + s_im * r_re], axis=1)
    pos_grad = jax.nn.sigmoid(jnp.sum(query * target, axis=1)) - 1.0
    query_bf = query.astype(jnp.bfloat16)
    weight = 1.0 / math.sqrt(n_blk * negatives)
    neg_score = lax.dot_general(
        query_bf, spans, (((1,), (1,)), ((), ())), preferred_element_type=jnp.float32
    )
    neg_grad = (weight * jax.nn.sigmoid(neg_score)).astype(jnp.bfloat16)
    query_grad = pos_grad[:, None] * target + jnp.dot(
        neg_grad, spans, preferred_element_type=jnp.float32
    )
    span_part = lax.dot_general(
        neg_grad, query_bf, (((0,), (0,)), ((), ())), preferred_element_type=jnp.float32
    ).reshape(n_blk, negatives, width)
    carried = span_part[0]
    for d in range(1, n_blk):
        carried = carried + shifted(span_part[d], "blk", n_blk, -d)
    q_re, q_im = (query_grad[:, :half], query_grad[:, half:])
    source_grad = jnp.concatenate([q_re * r_re + q_im * r_im, q_im * r_re - q_re * r_im], axis=1)
    rel_term = jnp.concatenate([q_re * s_re + q_im * s_im, q_im * s_re - q_re * s_im], axis=1)
    target_grad = pos_grad[:, None] * query

    rel_rows_n = relation.shape[0]
    total = rel_rows_n * width
    per_peer = -(-total // (n_blk * n_shard * LANE)) * LANE
    local_relation = jnp.zeros((rel_rows_n, width), jnp.float32).at[rel_ids].add(rel_term)
    quarters = jnp.pad(local_relation.reshape(-1), (0, n_blk * n_shard * per_peer - total))
    quarters = quarters.reshape(n_blk, n_shard, per_peer)
    mine = lax.dynamic_index_in_dim(quarters, me_blk, 0, keepdims=False)
    for d in range(1, n_blk):
        outgoing_quarter = lax.dynamic_index_in_dim(quarters, (me_blk + d) % n_blk, 0, keepdims=False)
        mine = mine + shifted(outgoing_quarter, "blk", n_blk, d)

    small = lax.all_to_all(
        mine.reshape(n_shard, 1, per_peer), "shard", 0, 0, tiled=True
    ).sum(axis=(0, 1))
    quarter = spread(small, "shard", n_shard)
    held = jnp.stack([quarter] + [shifted(quarter, "blk", n_blk, d) for d in range(1, n_blk)])
    order = (me_blk - jnp.arange(n_blk, dtype=jnp.int32)) % n_blk
    relation_grad = jnp.take(held, order, axis=0).reshape(-1)[:total].reshape(rel_rows_n, width)

    sub = 8
    grad_lanes = capacity * width // sub
    outgoing = (
        jnp.zeros((n_shard * capacity, width), jnp.float32)
        .at[source_slots]
        .set(source_grad)
        .at[target_slots]
        .set(target_grad)
    )
    payload = outgoing.reshape(n_shard, sub, grad_lanes)
    arrived = lax.all_to_all(payload, "shard", split_axis=0, concat_axis=0, tiled=True)
    arrived_grads = arrived.reshape(n_shard * capacity, width)

    entity_grad = (
        jnp.zeros((rows_own, width), jnp.float32)
        .at[asked_rows.reshape(-1)]
        .add(arrived_grads)
    )
    current = lax.dynamic_slice_in_dim(entity_grad, span_start, negatives, 0)
    entity_grad = lax.dynamic_update_slice_in_dim(entity_grad, current + carried, span_start, 0)
    return (entity_grad, relation_grad)


def solution(mesh):
    in_specs = (
        P(("blk", "shard"), None),
        P(),
        P(("blk", "shard"), None),
        P(("blk", "shard"), None),
        P(("blk", "shard")),
        P(("blk", "shard")),
    )
    out_specs = (P(("blk", "shard"), None), P())
    return jax.shard_map(shards, mesh=mesh, in_specs=in_specs, out_specs=out_specs, check_vma=False)
```

```python
import math

import jax
import jax.numpy as jnp
from jax import lax
from jax.sharding import PartitionSpec as P

NEG = 1024
LANE = 128


def shifted(value, axis, n, by):
    return lax.ppermute(value, axis, [(i, (i + by) % n) for i in range(n)])


def spread(value, axis, n):
    copies = jnp.broadcast_to(value[None], (n,) + value.shape)
    return lax.all_to_all(copies, axis, 0, 0, tiled=False)


def owner_rank(flat_owner, n_shard):
    count = flat_owner.shape[0]
    onehot = flat_owner[:, None] == jnp.arange(n_shard, dtype=jnp.int32)[None, :]
    index = jnp.arange(count, dtype=jnp.int32)
    earlier = (index[:, None] > index[None, :]).astype(jnp.bfloat16)
    before = jnp.dot(earlier, onehot.astype(jnp.bfloat16), preferred_element_type=jnp.float32)
    return jnp.sum(jnp.where(onehot, before, 0.0), axis=1).astype(jnp.int32)


def shards(table, relation, owners, rows, rel_ids, span_ids):
    n_shard = lax.axis_size("shard")
    n_blk = lax.axis_size("blk")
    me_blk = lax.axis_index("blk")
    edges = owners.shape[0]
    rows_own = table.shape[0]
    width = table.shape[1]
    half = width // 2
    capacity = 4 * edges // n_shard
    negatives = NEG
    span_start = span_ids[0] * negatives
    span = lax.dynamic_slice_in_dim(table, span_start, negatives, 0)
    spans = jnp.concatenate(
        [span] + [shifted(span, "blk", n_blk, d) for d in range(1, n_blk)], axis=0
    )
    flat_owner = owners.reshape(-1)
    flat_row = rows.reshape(-1)
    ranking = owner_rank(flat_owner, n_shard)
    slots = flat_owner * capacity + ranking
    requests = (
        jnp.zeros((n_shard * capacity,), jnp.int32)
        .at[slots]
        .set(flat_row)
        .reshape(n_shard, capacity)
    )
    asked_rows = lax.all_to_all(requests, "shard", split_axis=0, concat_axis=0, tiled=True)
    fetched = lax.all_to_all(table[asked_rows], "shard", split_axis=0, concat_axis=0, tiled=True)
    fetched = fetched.reshape(n_shard * capacity, width)
    end_slots = slots.reshape(edges, 2)
    source_slots = end_slots[:, 0]
    target_slots = end_slots[:, 1]
    source = fetched[source_slots].astype(jnp.float32)
    target = fetched[target_slots].astype(jnp.float32)
    rel_rows = relation[rel_ids].astype(jnp.float32)
    s_re, s_im = (source[:, :half], source[:, half:])
    r_re, r_im = (rel_rows[:, :half], rel_rows[:, half:])
    query = jnp.concatenate([s_re * r_re - s_im * r_im, s_re * r_im + s_im * r_re], axis=1)
    pos_grad = jax.nn.sigmoid(jnp.sum(query * target, axis=1)) - 1.0
    query_bf = query.astype(jnp.bfloat16)
    weight = 1.0 / math.sqrt(n_blk * negatives)
    neg_score = lax.dot_general(
        query_bf, spans, (((1,), (1,)), ((), ())), preferred_element_type=jnp.float32
    )
    neg_grad = (weight * jax.nn.sigmoid(neg_score)).astype(jnp.bfloat16)
    query_grad = pos_grad[:, None] * target + jnp.dot(
        neg_grad, spans, preferred_element_type=jnp.float32
    )
    span_part = lax.dot_general(
        neg_grad, query_bf, (((0,), (0,)), ((), ())), preferred_element_type=jnp.float32
    ).reshape(n_blk, negatives, width)
    carried = span_part[0]
    for d in range(1, n_blk):
        carried = carried + shifted(span_part[d], "blk", n_blk, -d)
    q_re, q_im = (query_grad[:, :half], query_grad[:, half:])
    source_grad = jnp.concatenate([q_re * r_re + q_im * r_im, q_im * r_re - q_re * r_im], axis=1)
    rel_term = jnp.concatenate([q_re * s_re + q_im * s_im, q_im * s_re - q_re * s_im], axis=1)
    target_grad = pos_grad[:, None] * query

    rel_rows_n = relation.shape[0]
    total = rel_rows_n * width
    per_peer = -(-total // (n_blk * n_shard * LANE)) * LANE
    local_relation = jnp.zeros((rel_rows_n, width), jnp.float32).at[rel_ids].add(rel_term)
    quarters = jnp.pad(local_relation.reshape(-1), (0, n_blk * n_shard * per_peer - total))
    quarters = quarters.reshape(n_blk, n_shard, per_peer)
    mine = lax.dynamic_index_in_dim(quarters, me_blk, 0, keepdims=False)
    for d in range(1, n_blk):
        outgoing_quarter = lax.dynamic_index_in_dim(quarters, (me_blk + d) % n_blk, 0, keepdims=False)
        mine = mine + shifted(outgoing_quarter, "blk", n_blk, d)

    small = lax.all_to_all(
        mine.reshape(n_shard, 1, per_peer), "shard", 0, 0, tiled=True
    ).sum(axis=(0, 1))
    quarter = spread(small, "shard", n_shard)
    held = jnp.stack([quarter] + [shifted(quarter, "blk", n_blk, d) for d in range(1, n_blk)])
    order = (me_blk - jnp.arange(n_blk, dtype=jnp.int32)) % n_blk
    relation_grad = jnp.take(held, order, axis=0).reshape(-1)[:total].reshape(rel_rows_n, width)

    sub = 8
    grad_lanes = capacity * width // sub
    outgoing = (
        jnp.zeros((n_shard * capacity, width), jnp.float32)
        .at[source_slots]
        .set(source_grad)
        .at[target_slots]
        .set(target_grad)
    )
    payload = outgoing.reshape(n_shard, sub, grad_lanes)
    arrived = lax.all_to_all(payload, "shard", split_axis=0, concat_axis=0, tiled=True)
    arrived_grads = arrived.reshape(n_shard * capacity, width)

    base = lax.dynamic_update_slice_in_dim(
        jnp.zeros((rows_own, width), jnp.float32), carried, span_start, 0
    )
    entity_grad = base.at[asked_rows.reshape(-1)].add(arrived_grads)
    return (entity_grad, relation_grad)


def solution(mesh):
    in_specs = (
        P(("blk", "shard"), None),
        P(),
        P(("blk", "shard"), None),
        P(("blk", "shard"), None),
        P(("blk", "shard")),
        P(("blk", "shard")),
    )
    out_specs = (P(("blk", "shard"), None), P())
    return jax.shard_map(shards, mesh=mesh, in_specs=in_specs, out_specs=out_specs, check_vma=False)
```

```python
import math

import jax
import jax.numpy as jnp
from jax import lax
from jax.sharding import PartitionSpec as P

NEG = 1024
LANE = 128


def shifted(value, axis, n, by):
    return lax.ppermute(value, axis, [(i, (i + by) % n) for i in range(n)])


def spread(value, axis, n):
    copies = jnp.broadcast_to(value[None], (n,) + value.shape)
    return lax.all_to_all(copies, axis, 0, 0, tiled=False)


def owner_rank(flat_owner, n_shard):
    count = flat_owner.shape[0]
    onehot = flat_owner[:, None] == jnp.arange(n_shard, dtype=jnp.int32)[None, :]
    index = jnp.arange(count, dtype=jnp.int32)
    earlier = (index[:, None] > index[None, :]).astype(jnp.bfloat16)
    before = jnp.dot(earlier, onehot.astype(jnp.bfloat16), preferred_element_type=jnp.float32)
    return jnp.sum(jnp.where(onehot, before, 0.0), axis=1).astype(jnp.int32)


def shards(table, relation, owners, rows, rel_ids, span_ids):
    n_shard = lax.axis_size("shard")
    n_blk = lax.axis_size("blk")
    me_blk = lax.axis_index("blk")
    edges = owners.shape[0]
    rows_own = table.shape[0]
    width = table.shape[1]
    half = width // 2
    capacity = 4 * edges // n_shard
    negatives = NEG
    span_start = span_ids[0] * negatives
    span = lax.dynamic_slice_in_dim(table, span_start, negatives, 0)
    spans = jnp.concatenate(
        [span] + [shifted(span, "blk", n_blk, d) for d in range(1, n_blk)], axis=0
    )
    flat_owner = owners.reshape(-1)
    flat_row = rows.reshape(-1)
    ranking = owner_rank(flat_owner, n_shard)
    slots = flat_owner * capacity + ranking
    requests = (
        jnp.zeros((n_shard * capacity,), jnp.int32)
        .at[slots]
        .set(flat_row)
        .reshape(n_shard, capacity)
    )
    asked_rows = lax.all_to_all(requests, "shard", split_axis=0, concat_axis=0, tiled=True)
    fetched = lax.all_to_all(table[asked_rows], "shard", split_axis=0, concat_axis=0, tiled=True)
    fetched = fetched.reshape(n_shard * capacity, width)
    end_slots = slots.reshape(edges, 2)
    source_slots = end_slots[:, 0]
    target_slots = end_slots[:, 1]
    source = fetched[source_slots].astype(jnp.float32)
    target = fetched[target_slots].astype(jnp.float32)
    rel_rows = relation[rel_ids].astype(jnp.float32)
    s_re, s_im = (source[:, :half], source[:, half:])
    r_re, r_im = (rel_rows[:, :half], rel_rows[:, half:])
    query = jnp.concatenate([s_re * r_re - s_im * r_im, s_re * r_im + s_im * r_re], axis=1)
    pos_grad = jax.nn.sigmoid(jnp.sum(query * target, axis=1)) - 1.0
    query_bf = query.astype(jnp.bfloat16)
    weight = 1.0 / math.sqrt(n_blk * negatives)
    neg_score = lax.dot_general(
        query_bf, spans, (((1,), (1,)), ((), ())), preferred_element_type=jnp.float32
    )
    neg_grad = (weight * jax.nn.sigmoid(neg_score)).astype(jnp.bfloat16)
    query_grad = pos_grad[:, None] * target + jnp.dot(
        neg_grad, spans, preferred_element_type=jnp.float32
    )
    span_part = lax.dot_general(
        neg_grad, query_bf, (((0,), (0,)), ((), ())), preferred_element_type=jnp.float32
    ).reshape(n_blk, negatives, width)
    carried = span_part[0]
    for d in range(1, n_blk):
        carried = carried + shifted(span_part[d], "blk", n_blk, -d)
    q_re, q_im = (query_grad[:, :half], query_grad[:, half:])
    source_grad = jnp.concatenate([q_re * r_re + q_im * r_im, q_im * r_re - q_re * r_im], axis=1)
    rel_term = jnp.concatenate([q_re * s_re + q_im * s_im, q_im * s_re - q_re * s_im], axis=1)
    target_grad = pos_grad[:, None] * query

    rel_rows_n = relation.shape[0]
    total = rel_rows_n * width
    per_peer = -(-total // (n_blk * n_shard * LANE)) * LANE
    local_relation = jnp.zeros((rel_rows_n, width), jnp.float32).at[rel_ids].add(rel_term)
    quarters = jnp.pad(local_relation.reshape(-1), (0, n_blk * n_shard * per_peer - total))
    quarters = quarters.reshape(n_blk, n_shard, per_peer)
    received = []
    for d in range(1, n_blk):
        outgoing_quarter = lax.dynamic_index_in_dim(quarters, (me_blk + d) % n_blk, 0, keepdims=False)
        received.append(shifted(outgoing_quarter, "blk", n_blk, d))
    outgoing = (
        jnp.zeros((n_shard * capacity, width), jnp.float32)
        .at[source_slots]
        .set(source_grad)
        .at[target_slots]
        .set(target_grad)
    )
    received, outgoing = lax.optimization_barrier((received, outgoing))
    mine = lax.dynamic_index_in_dim(quarters, me_blk, 0, keepdims=False)
    for part in received:
        mine = mine + part

    small = lax.all_to_all(
        mine.reshape(n_shard, 1, per_peer), "shard", 0, 0, tiled=True
    ).sum(axis=(0, 1))
    quarter = spread(small, "shard", n_shard)
    held = jnp.stack([quarter] + [shifted(quarter, "blk", n_blk, d) for d in range(1, n_blk)])
    order = (me_blk - jnp.arange(n_blk, dtype=jnp.int32)) % n_blk
    relation_grad = jnp.take(held, order, axis=0).reshape(-1)[:total].reshape(rel_rows_n, width)

    sub = 8
    grad_lanes = capacity * width // sub
    payload = outgoing.reshape(n_shard, sub, grad_lanes)
    arrived = lax.all_to_all(payload, "shard", split_axis=0, concat_axis=0, tiled=True)
    arrived_grads = arrived.reshape(n_shard * capacity, width)

    base = lax.dynamic_update_slice_in_dim(
        jnp.zeros((rows_own, width), jnp.float32), carried, span_start, 0
    )
    entity_grad = base.at[asked_rows.reshape(-1)].add(arrived_grads)
    return (entity_grad, relation_grad)


def solution(mesh):
    in_specs = (
        P(("blk", "shard"), None),
        P(),
        P(("blk", "shard"), None),
        P(("blk", "shard"), None),
        P(("blk", "shard")),
        P(("blk", "shard")),
    )
    out_specs = (P(("blk", "shard"), None), P())
    return jax.shard_map(shards, mesh=mesh, in_specs=in_specs, out_specs=out_specs, check_vma=False)
```

```python
import math

import jax
import jax.numpy as jnp
from jax import lax
from jax.sharding import PartitionSpec as P

NEG = 1024
LANE = 128


def shifted(value, axis, n, by):
    return lax.ppermute(value, axis, [(i, (i + by) % n) for i in range(n)])


def spread(value, axis, n):
    copies = jnp.broadcast_to(value[None], (n,) + value.shape)
    return lax.all_to_all(copies, axis, 0, 0, tiled=False)


def owner_rank(flat_owner, n_shard):
    count = flat_owner.shape[0]
    onehot = flat_owner[:, None] == jnp.arange(n_shard, dtype=jnp.int32)[None, :]
    index = jnp.arange(count, dtype=jnp.int32)
    earlier = (index[:, None] > index[None, :]).astype(jnp.bfloat16)
    before = jnp.dot(earlier, onehot.astype(jnp.bfloat16), preferred_element_type=jnp.float32)
    return jnp.sum(jnp.where(onehot, before, 0.0), axis=1).astype(jnp.int32)


def shards(table, relation, owners, rows, rel_ids, span_ids):
    n_shard = lax.axis_size("shard")
    n_blk = lax.axis_size("blk")
    me_blk = lax.axis_index("blk")
    edges = owners.shape[0]
    rows_own = table.shape[0]
    width = table.shape[1]
    half = width // 2
    capacity = 4 * edges // n_shard
    negatives = NEG
    span_start = span_ids[0] * negatives
    span = lax.dynamic_slice_in_dim(table, span_start, negatives, 0)
    spans = jnp.concatenate(
        [span] + [shifted(span, "blk", n_blk, d) for d in range(1, n_blk)], axis=0
    )
    flat_owner = owners.reshape(-1)
    flat_row = rows.reshape(-1)
    ranking = owner_rank(flat_owner, n_shard)
    slots = flat_owner * capacity + ranking
    requests = (
        jnp.zeros((n_shard * capacity,), jnp.int32)
        .at[slots]
        .set(flat_row)
        .reshape(n_shard, capacity)
    )
    asked_rows = lax.all_to_all(requests, "shard", split_axis=0, concat_axis=0, tiled=True)
    fetched = lax.all_to_all(table[asked_rows], "shard", split_axis=0, concat_axis=0, tiled=True)
    fetched = fetched.reshape(n_shard * capacity, width)
    end_slots = slots.reshape(edges, 2)
    source_slots = end_slots[:, 0]
    target_slots = end_slots[:, 1]
    source = fetched[source_slots].astype(jnp.float32)
    target = fetched[target_slots].astype(jnp.float32)
    rel_rows = relation[rel_ids].astype(jnp.float32)
    s_re, s_im = (source[:, :half], source[:, half:])
    r_re, r_im = (rel_rows[:, :half], rel_rows[:, half:])
    query = jnp.concatenate([s_re * r_re - s_im * r_im, s_re * r_im + s_im * r_re], axis=1)
    pos_grad = jax.nn.sigmoid(jnp.sum(query * target, axis=1)) - 1.0
    query_bf = query.astype(jnp.bfloat16)
    weight = 1.0 / math.sqrt(n_blk * negatives)
    neg_score = lax.dot_general(
        query_bf, spans, (((1,), (1,)), ((), ())), preferred_element_type=jnp.float32
    )
    neg_grad = (weight * jax.nn.sigmoid(neg_score)).astype(jnp.bfloat16)
    query_grad = pos_grad[:, None] * target + jnp.dot(
        neg_grad, spans, preferred_element_type=jnp.float32
    )
    span_part = lax.dot_general(
        neg_grad, query_bf, (((0,), (0,)), ((), ())), preferred_element_type=jnp.float32
    ).reshape(n_blk, negatives, width)
    carried = span_part[0]
    for d in range(1, n_blk):
        carried = carried + shifted(span_part[d], "blk", n_blk, -d)
    q_re, q_im = (query_grad[:, :half], query_grad[:, half:])
    source_grad = jnp.concatenate([q_re * r_re + q_im * r_im, q_im * r_re - q_re * r_im], axis=1)
    rel_term = jnp.concatenate([q_re * s_re + q_im * s_im, q_im * s_re - q_re * s_im], axis=1)
    target_grad = pos_grad[:, None] * query

    rel_rows_n = relation.shape[0]
    total = rel_rows_n * width
    per_peer = -(-total // (n_blk * n_shard * LANE)) * LANE
    local_relation = jnp.zeros((rel_rows_n, width), jnp.float32).at[rel_ids].add(rel_term)
    quarters = jnp.pad(local_relation.reshape(-1), (0, n_blk * n_shard * per_peer - total))
    quarters = quarters.reshape(n_blk, n_shard, per_peer)
    received = []
    for d in range(1, n_blk):
        outgoing_quarter = lax.dynamic_index_in_dim(quarters, (me_blk + d) % n_blk, 0, keepdims=False)
        received.append(shifted(outgoing_quarter, "blk", n_blk, d))
    outgoing = (
        jnp.zeros((n_shard * capacity, width), jnp.float32)
        .at[source_slots]
        .set(source_grad)
        .at[target_slots]
        .set(target_grad)
    )
    received, outgoing = lax.optimization_barrier((received, outgoing))
    mine = lax.dynamic_index_in_dim(quarters, me_blk, 0, keepdims=False)
    for part in received:
        mine = mine + part

    quarter = lax.psum(mine, "shard")
    held = jnp.stack([quarter] + [shifted(quarter, "blk", n_blk, d) for d in range(1, n_blk)])
    order = (me_blk - jnp.arange(n_blk, dtype=jnp.int32)) % n_blk
    relation_grad = jnp.take(held, order, axis=0).reshape(-1)[:total].reshape(rel_rows_n, width)

    sub = 8
    grad_lanes = capacity * width // sub
    payload = outgoing.reshape(n_shard, sub, grad_lanes)
    arrived = lax.all_to_all(payload, "shard", split_axis=0, concat_axis=0, tiled=True)
    arrived_grads = arrived.reshape(n_shard * capacity, width)

    base = lax.dynamic_update_slice_in_dim(
        jnp.zeros((rows_own, width), jnp.float32), carried, span_start, 0
    )
    entity_grad = base.at[asked_rows.reshape(-1)].add(arrived_grads)
    return (entity_grad, relation_grad)


def solution(mesh):
    in_specs = (
        P(("blk", "shard"), None),
        P(),
        P(("blk", "shard"), None),
        P(("blk", "shard"), None),
        P(("blk", "shard")),
        P(("blk", "shard")),
    )
    out_specs = (P(("blk", "shard"), None), P())
    return jax.shard_map(shards, mesh=mesh, in_specs=in_specs, out_specs=out_specs, check_vma=False)
```

```python
import math

import jax
import jax.numpy as jnp
from jax import lax
from jax.sharding import PartitionSpec as P

NEG = 1024
LANE = 128


def shifted(value, axis, n, by):
    return lax.ppermute(value, axis, [(i, (i + by) % n) for i in range(n)])


def spread(value, axis, n):
    copies = jnp.broadcast_to(value[None], (n,) + value.shape)
    return lax.all_to_all(copies, axis, 0, 0, tiled=False)


def owner_rank(flat_owner, n_shard):
    count = flat_owner.shape[0]
    onehot = flat_owner[:, None] == jnp.arange(n_shard, dtype=jnp.int32)[None, :]
    index = jnp.arange(count, dtype=jnp.int32)
    earlier = (index[:, None] > index[None, :]).astype(jnp.bfloat16)
    before = jnp.dot(earlier, onehot.astype(jnp.bfloat16), preferred_element_type=jnp.float32)
    return jnp.sum(jnp.where(onehot, before, 0.0), axis=1).astype(jnp.int32)


def shards(table, relation, owners, rows, rel_ids, span_ids):
    n_shard = lax.axis_size("shard")
    n_blk = lax.axis_size("blk")
    me_blk = lax.axis_index("blk")
    edges = owners.shape[0]
    rows_own = table.shape[0]
    width = table.shape[1]
    half = width // 2
    capacity = 4 * edges // n_shard
    negatives = NEG
    span_start = span_ids[0] * negatives
    span = lax.dynamic_slice_in_dim(table, span_start, negatives, 0)
    spans = jnp.concatenate(
        [span] + [shifted(span, "blk", n_blk, d) for d in range(1, n_blk)], axis=0
    )
    flat_owner = owners.reshape(-1)
    flat_row = rows.reshape(-1)
    ranking = owner_rank(flat_owner, n_shard)
    slots = flat_owner * capacity + ranking
    requests = (
        jnp.zeros((n_shard * capacity,), jnp.int32)
        .at[slots]
        .set(flat_row)
        .reshape(n_shard, capacity)
    )
    asked_rows = lax.all_to_all(requests, "shard", split_axis=0, concat_axis=0, tiled=True)
    picks = asked_rows.reshape(-1, 1) == jnp.arange(rows_own, dtype=jnp.int32)[None, :]
    asked_table = jnp.dot(
        picks.astype(jnp.bfloat16), table, preferred_element_type=jnp.float32
    ).astype(jnp.bfloat16).reshape(n_shard, capacity, width)
    fetched = lax.all_to_all(asked_table, "shard", split_axis=0, concat_axis=0, tiled=True)
    fetched = fetched.reshape(n_shard * capacity, width)
    end_slots = slots.reshape(edges, 2)
    source_slots = end_slots[:, 0]
    target_slots = end_slots[:, 1]
    source = fetched[source_slots].astype(jnp.float32)
    target = fetched[target_slots].astype(jnp.float32)
    rel_rows = relation[rel_ids].astype(jnp.float32)
    s_re, s_im = (source[:, :half], source[:, half:])
    r_re, r_im = (rel_rows[:, :half], rel_rows[:, half:])
    query = jnp.concatenate([s_re * r_re - s_im * r_im, s_re * r_im + s_im * r_re], axis=1)
    pos_grad = jax.nn.sigmoid(jnp.sum(query * target, axis=1)) - 1.0
    query_bf = query.astype(jnp.bfloat16)
    weight = 1.0 / math.sqrt(n_blk * negatives)
    neg_score = lax.dot_general(
        query_bf, spans, (((1,), (1,)), ((), ())), preferred_element_type=jnp.float32
    )
    neg_grad = (weight * jax.nn.sigmoid(neg_score)).astype(jnp.bfloat16)
    query_grad = pos_grad[:, None] * target + jnp.dot(
        neg_grad, spans, preferred_element_type=jnp.float32
    )
    span_part = lax.dot_general(
        neg_grad, query_bf, (((0,), (0,)), ((), ())), preferred_element_type=jnp.float32
    ).reshape(n_blk, negatives, width)
    carried = span_part[0]
    for d in range(1, n_blk):
        carried = carried + shifted(span_part[d], "blk", n_blk, -d)
    q_re, q_im = (query_grad[:, :half], query_grad[:, half:])
    source_grad = jnp.concatenate([q_re * r_re + q_im * r_im, q_im * r_re - q_re * r_im], axis=1)
    rel_term = jnp.concatenate([q_re * s_re + q_im * s_im, q_im * s_re - q_re * s_im], axis=1)
    target_grad = pos_grad[:, None] * query

    rel_rows_n = relation.shape[0]
    total = rel_rows_n * width
    per_peer = -(-total // (n_blk * n_shard * LANE)) * LANE
    local_relation = jnp.zeros((rel_rows_n, width), jnp.float32).at[rel_ids].add(rel_term)
    quarters = jnp.pad(local_relation.reshape(-1), (0, n_blk * n_shard * per_peer - total))
    quarters = quarters.reshape(n_blk, n_shard, per_peer)
    received = []
    for d in range(1, n_blk):
        outgoing_quarter = lax.dynamic_index_in_dim(quarters, (me_blk + d) % n_blk, 0, keepdims=False)
        received.append(shifted(outgoing_quarter, "blk", n_blk, d))
    outgoing = (
        jnp.zeros((n_shard * capacity, width), jnp.float32)
        .at[source_slots]
        .set(source_grad)
        .at[target_slots]
        .set(target_grad)
    )
    received, outgoing = lax.optimization_barrier((received, outgoing))
    mine = lax.dynamic_index_in_dim(quarters, me_blk, 0, keepdims=False)
    for part in received:
        mine = mine + part

    small = lax.all_to_all(
        mine.reshape(n_shard, 1, per_peer), "shard", 0, 0, tiled=True
    ).sum(axis=(0, 1))
    quarter = spread(small, "shard", n_shard)
    held = jnp.stack([quarter] + [shifted(quarter, "blk", n_blk, d) for d in range(1, n_blk)])
    order = (me_blk - jnp.arange(n_blk, dtype=jnp.int32)) % n_blk
    relation_grad = jnp.take(held, order, axis=0).reshape(-1)[:total].reshape(rel_rows_n, width)

    sub = 8
    grad_lanes = capacity * width // sub
    payload = outgoing.reshape(n_shard, sub, grad_lanes)
    arrived = lax.all_to_all(payload, "shard", split_axis=0, concat_axis=0, tiled=True)
    arrived_grads = arrived.reshape(n_shard * capacity, width)

    base = lax.dynamic_update_slice_in_dim(
        jnp.zeros((rows_own, width), jnp.float32), carried, span_start, 0
    )
    entity_grad = base.at[asked_rows.reshape(-1)].add(arrived_grads)
    return (entity_grad, relation_grad)


def solution(mesh):
    in_specs = (
        P(("blk", "shard"), None),
        P(),
        P(("blk", "shard"), None),
        P(("blk", "shard"), None),
        P(("blk", "shard")),
        P(("blk", "shard")),
    )
    out_specs = (P(("blk", "shard"), None), P())
    return jax.shard_map(shards, mesh=mesh, in_specs=in_specs, out_specs=out_specs, check_vma=False)
```
